512 devices in a mesh: gx: 64 (over z, y_lo, core), gz: 8 (over x, y_hi).
Axes of the slice: x: 4, y: 4 (y_hi: 2, y_lo: 2; y = y_hi * 2 + y_lo), z: 16, core: 2. Of those that a mesh axis runs over, the one named last changes fastest.
Arguments:
- adjoint: bfloat16 [3, 512, 256, 256], P(None, 'gx', 'gz'), may hold values from -6 to 6
- strain: bfloat16 [512, 256, 256], P('gx', 'gz'), may hold values from -16 to 16
- correction: float32 [256, 256], P('gz'), may hold values from 0.3 to 3
- metric: float32 [256], replicated, may hold values from 0.5 to 4
- stream_inverse: bfloat16 [512, 512], replicated, may hold values from -0.081 to 1.081
- span_inverse: bfloat16 [256, 256], replicated, may hold values from -0.081 to 1.081
- wall_operator: bfloat16 [256, 256], replicated, may hold values from -0.081 to 1.081
Outputs:
- adjoint_next: bfloat16 [3, 512, 256, 256], P(None, 'gx', 'gz')
- gradient: float32 [256, 256], P('gz', 'gx')
The draws below stay inside these ranges and needn't reach their ends.
All inputs are finite; a program needn't handle non-finite values.
Results may differ from the reference program's by a relative error of at most 0.013.
Values may be sent and summed in bfloat16 or wider, within the bound.
No kernel may reach another device: no remote copies, remote signals or barrier semaphores. Data moves between devices by JAX's collectives and lax.ppermute only.
A program may use at most 64 MiB of HBM per device.

```python
import math
import jax
import jax.numpy as jnp
from jax import lax

NY = 256
NX = 512
NZ = 256


def inverse_block(key, order):
    spread = jax.random.uniform(key, (order, order), jnp.float32, -0.08, 0.08)
    return spread + jnp.eye(order, dtype=jnp.float32)


def draw_stream_inverse(key, part):
    return inverse_block(jax.random.fold_in(key, 11), NX).astype(jnp.bfloat16)


def draw_span_inverse(key, part):
    return inverse_block(jax.random.fold_in(key, 23), NZ).astype(jnp.bfloat16)


def draw_wall_operator(key, part):
    return inverse_block(jax.random.fold_in(key, 37), NY).astype(jnp.bfloat16)


def strengthened(values, own_key, source, target, blocks, factor):
    owner, partner = [(jnp.arange(values.shape[position]) // (values.shape[position] // blocks)).reshape([-1 if axis == position else 1 for axis in range(values.ndim)]) for position in (source, target)]
    chosen = jax.random.permutation(own_key, blocks)[partner]
    strong = (owner == chosen) | (owner == (partner + blocks // 2) % blocks)
    return jnp.where(strong, factor * values, values)


def level_of(own_key, shape, shards, smallest, top_value):
    factor_of, own = 1.0, jax.random.fold_in(own_key, 6)
    for position, blocks in shards:
        steps = jnp.exp(jax.random.uniform(jax.random.fold_in(own, position), (blocks,), jnp.float32, smallest / len(shards), top_value / len(shards)))
        factor_of = factor_of * jnp.repeat(steps, shape[position] // blocks).reshape([-1 if axis == position else 1 for axis in range(len(shape))])
    return factor_of


def noise(rng, shape, scale, most, cuts=(), kind=jnp.bfloat16):
    loudness = level_of(rng, shape, cuts, -0.22, 0.18) if cuts else 1.0
    drawn = jax.random.normal(rng, shape, jnp.float32) * scale * loudness
    return jnp.minimum(jnp.maximum(drawn, -most), most).astype(kind)


def bell_draw_with(own_key, shape, deviation, reach, split, heavy, kind=jnp.bfloat16):
    array = deviation * jax.random.normal(own_key, shape, jnp.float32)
    if split:
        array = array * level_of(own_key, shape, split, -0.22, 0.18)
    return jnp.clip(strengthened(array, jax.random.fold_in(own_key, 3), *heavy), -reach, reach).astype(kind)


def setup_inputs(seed: int = 0) -> dict:
    streams_of = jax.random.split(jax.random.key(seed), 8)
    return {
        "adjoint": noise(streams_of[0], (3, NX, NZ, NY), 1.0, 6.0, ((1, 64), (2, 8))),
        "strain": bell_draw_with(streams_of[1], (NX, NZ, NY), 1.0, 16.0, ((0, 64), (1, 8)), (0, 2, 64, 4.0)),
        "correction": jnp.clip(jnp.exp(math.log(3.0) - 2.3025851 * jax.random.uniform(streams_of[2], (NZ, NY), jnp.float32) ** level_of(streams_of[2], (NZ, NY), ((0, 8),), -0.2, 0.2)), 0.3, 3.0),
        "metric": jnp.clip(jnp.exp(jax.random.uniform(streams_of[3], (NY,), jnp.float32, math.log(0.5), math.log(4.0))), 0.5, 4.0),
        "stream_inverse": draw_stream_inverse(jax.random.fold_in(streams_of[7], 71), 0),
        "span_inverse": draw_span_inverse(jax.random.fold_in(streams_of[7], 71), 0),
        "wall_operator": draw_wall_operator(jax.random.fold_in(streams_of[7], 71), 0),
    }


near_coef = 7.0 / 9.0
far_coef = 1.0 / 36.0
time_step = 0.25


def stencil(source, axis):
    widened = source.astype(jnp.float32)
    near_diff = jnp.roll(widened, -1, axis) - jnp.roll(widened, 1, axis)
    far_diff = jnp.roll(widened, -2, axis) - jnp.roll(widened, 2, axis)
    return (near_coef * near_diff + far_coef * far_diff).astype(jnp.bfloat16)


def reference(adjoint, strain, correction, metric, stream_inverse, span_inverse, wall_operator):
    strain_wide = strain.astype(jnp.float32)
    viscosity = (correction[None] * strain_wide).astype(jnp.bfloat16)
    viscous = viscosity.astype(jnp.float32)
    stream_wide = stream_inverse.astype(jnp.float32)
    span_wide = span_inverse.astype(jnp.float32)
    wall_wide = wall_operator.astype(jnp.float32)

    def stream_derivative(source):
        right_side = stencil(source, 0).astype(jnp.float32)
        return jnp.einsum('ij,jzy->izy', stream_wide, right_side).astype(jnp.bfloat16)

    def span_derivative(source):
        right_side = stencil(source, 1).astype(jnp.float32)
        return jnp.einsum('ij,xjy->xiy', span_wide, right_side).astype(jnp.bfloat16)

    def wall_derivative(source):
        return jnp.einsum('xzj,ij->xzi', source.astype(jnp.float32), wall_wide) * metric

    def per_component(source):
        stream_grad = stream_derivative(source)
        wall_grad = wall_derivative(source).astype(jnp.bfloat16)
        span_grad = span_derivative(source)
        stream_flux = (viscous * stream_grad.astype(jnp.float32)).astype(jnp.bfloat16)
        wall_flux = (viscous * wall_grad.astype(jnp.float32)).astype(jnp.bfloat16)
        span_flux = (viscous * span_grad.astype(jnp.float32)).astype(jnp.bfloat16)
        total = stream_derivative(stream_flux).astype(jnp.float32) + wall_derivative(wall_flux)
        total = total + span_derivative(span_flux).astype(jnp.float32)
        updated = (source.astype(jnp.float32) + time_step * total).astype(jnp.bfloat16)
        squares = stream_grad.astype(jnp.float32) ** 2 + wall_grad.astype(jnp.float32) ** 2
        squares = squares + span_grad.astype(jnp.float32) ** 2
        return updated, jnp.sum(strain_wide * squares, axis=0)

    new_fields, dissipation = lax.map(per_component, adjoint)
    gradient = -jnp.sum(dissipation, axis=0) / NX
    return new_fields, gradient
```

```python
import jax
import jax.numpy as jnp
from jax import lax
from jax.sharding import PartitionSpec as P

near_coef = 7.0 / 9.0
far_coef = 1.0 / 36.0
time_step = 0.25


def stencil(source, axis):
    widened = source.astype(jnp.float32)
    near_diff = jnp.roll(widened, -1, axis) - jnp.roll(widened, 1, axis)
    far_diff = jnp.roll(widened, -2, axis) - jnp.roll(widened, 2, axis)
    return (near_coef * near_diff + far_coef * far_diff).astype(jnp.bfloat16)


def stream_derivative(pencil, stream_inverse):
    right_side = stencil(pencil, 1)
    product = jnp.einsum(
        "ij,kjp->kip", stream_inverse, right_side, preferred_element_type=jnp.float32
    )
    return product.astype(jnp.bfloat16)


def span_derivative(pencil, span_inverse):
    right_side = stencil(pencil, 2)
    product = jnp.einsum(
        "ij,kajy->kaiy", span_inverse, right_side, preferred_element_type=jnp.float32
    )
    return product.astype(jnp.bfloat16)


def wall_derivative(source, wall_operator, metric):
    product = jnp.einsum("kxzj,ij->kxzi", source, wall_operator, preferred_element_type=jnp.float32)
    return product * metric


def stream_apply(source, stream_inverse):
    flat_source = source.reshape(source.shape[0], source.shape[1], -1)
    derived = stream_derivative(
        lax.all_to_all(flat_source, "gx", split_axis=2, concat_axis=1, tiled=True), stream_inverse
    )
    result = lax.all_to_all(derived, "gx", split_axis=1, concat_axis=2, tiled=True)
    return result.reshape(source.shape)


def span_apply(source, span_inverse):
    derived = span_derivative(
        lax.all_to_all(source, "gz", split_axis=1, concat_axis=2, tiled=True), span_inverse
    )
    return lax.all_to_all(derived, "gz", split_axis=2, concat_axis=1, tiled=True)


def on_device(adjoint, strain, correction, metric, stream_inverse, span_inverse, wall_operator):
    components, stream_cells, span_cells, wall_cells = adjoint.shape
    strain_wide = strain.astype(jnp.float32)
    viscosity = (correction[None] * strain_wide).astype(jnp.bfloat16)
    viscous = viscosity.astype(jnp.float32)[None]
    stream_grad = stream_apply(adjoint, stream_inverse)
    stream_flux = (viscous * stream_grad.astype(jnp.float32)).astype(jnp.bfloat16)
    stream_diverge = stream_apply(stream_flux, stream_inverse)
    span_grad = span_apply(adjoint, span_inverse)
    span_flux = (viscous * span_grad.astype(jnp.float32)).astype(jnp.bfloat16)
    span_diverge = span_apply(span_flux, span_inverse)
    wall_grad = wall_derivative(adjoint, wall_operator, metric).astype(jnp.bfloat16)
    wall_flux = (viscous * wall_grad.astype(jnp.float32)).astype(jnp.bfloat16)
    wall_diverge = wall_derivative(wall_flux, wall_operator, metric)
    total = stream_diverge.astype(jnp.float32) + wall_diverge + span_diverge.astype(jnp.float32)
    updated = (adjoint.astype(jnp.float32) + time_step * total).astype(jnp.bfloat16)
    squares = stream_grad.astype(jnp.float32) ** 2 + wall_grad.astype(jnp.float32) ** 2
    squares = jnp.sum(squares + span_grad.astype(jnp.float32) ** 2, axis=0)
    partial_sum = jnp.sum(strain_wide * squares, axis=0)
    groups = lax.axis_size("gx")
    pieces = partial_sum.reshape(span_cells, groups, wall_cells // groups).transpose(1, 0, 2)
    pieces = lax.all_to_all(pieces.reshape(groups, -1), "gx", 0, 0, tiled=True)
    summed = jnp.sum(pieces, axis=0).reshape(span_cells, wall_cells // groups)
    gradient = -summed / (stream_cells * lax.axis_size("gx"))
    return (updated, gradient)


def solution(mesh):
    in_specs = (P(None, "gx", "gz", None), P("gx", "gz", None), P("gz", None), P(), P(), P(), P())
    out_specs = (P(None, "gx", "gz", None), P("gz", "gx"))
    return jax.shard_map(
        on_device, mesh=mesh, in_specs=in_specs, out_specs=out_specs, check_vma=False
    )
```

```python
import jax
import jax.numpy as jnp
from jax import lax
from jax.sharding import PartitionSpec as P

near_coef = 7.0 / 9.0
far_coef = 1.0 / 36.0
time_step = 0.25
f32 = jnp.float32
bf16 = jnp.bfloat16


def stencil(source, axis):
    widened = source.astype(f32)
    near_diff = jnp.roll(widened, -1, axis) - jnp.roll(widened, 1, axis)
    far_diff = jnp.roll(widened, -2, axis) - jnp.roll(widened, 2, axis)
    return (near_coef * near_diff + far_coef * far_diff).astype(bf16)


def derivative(pencil, operator):
    right_side = stencil(pencil, 1)
    product = jnp.einsum("ij,cjp->cip", operator, right_side, preferred_element_type=f32)
    return product.astype(bf16)


def wall_derivative(source, wall_operator, metric):
    product = jnp.einsum("kxzj,ij->kxzi", source, wall_operator, preferred_element_type=f32)
    return product * metric


def on_device(adjoint, strain, correction, metric, stream_inverse, span_inverse, wall_operator):
    comps, nxl, nzl, ny = adjoint.shape
    gxn = lax.axis_size("gx")
    lanes = nzl * ny // gxn
    yparts = ny // lanes
    nx = nxl * gxn
    strain_wide = strain.astype(f32)
    viscosity = (correction[None] * strain_wide).astype(bf16)
    viscous = viscosity.astype(f32)

    xs = jnp.concatenate([adjoint, strain[None]], axis=0)
    xs = xs.reshape(comps + 1, nxl, nzl, yparts, lanes).transpose(2, 3, 0, 1, 4)
    xs = xs.reshape(gxn, comps + 1, nxl, lanes)
    xt = lax.all_to_all(xs, "gx", 0, 0, tiled=True)
    xt = xt.transpose(1, 0, 2, 3).reshape(comps + 1, nx, lanes)
    stream_strain = xt[comps].astype(f32)
    me = lax.axis_index("gx")
    z_at, y_at = me // yparts, (me % yparts) * lanes
    corr_row = lax.dynamic_slice(correction, (z_at, y_at), (1, lanes))
    stream_visc = (corr_row * stream_strain).astype(bf16).astype(f32)
    stream_grad = derivative(xt[:comps], stream_inverse)
    stream_flux = (stream_visc[None] * stream_grad.astype(f32)).astype(bf16)
    stream_div = derivative(stream_flux, stream_inverse)
    stream_sq = jnp.sum(stream_strain[None] * stream_grad.astype(f32) ** 2, axis=(0, 1))
    back = stream_div.reshape(comps, gxn, nxl, lanes).transpose(1, 0, 2, 3)
    back = lax.all_to_all(back, "gx", 0, 0, tiled=True)
    back = back.reshape(nzl, yparts, comps, nxl, lanes).transpose(2, 3, 0, 1, 4)
    stream_div = back.reshape(comps, nxl, nzl, ny)
    stream_part = lax.dynamic_update_slice(
        jnp.zeros((nzl, ny), f32), stream_sq[None], (z_at, y_at)
    )

    zs = jnp.concatenate([adjoint, viscosity[None], strain[None]], axis=0)
    zt = lax.all_to_all(zs, "gz", 1, 2, tiled=True)[:, 0]
    span_visc = zt[comps].astype(f32)
    span_strain = zt[comps + 1].astype(f32)
    span_grad = derivative(zt[:comps], span_inverse)
    span_flux = (span_visc[None] * span_grad.astype(f32)).astype(bf16)
    span_div = derivative(span_flux, span_inverse)
    span_sq = jnp.sum(span_strain[None] * span_grad.astype(f32) ** 2, axis=0)
    span_div = lax.all_to_all(span_div[:, None], "gz", 2, 1, tiled=True)
    span_part = jnp.sum(lax.all_to_all(span_sq[None], "gz", 1, 0, tiled=True), axis=0)

    wall_grad = wall_derivative(adjoint, wall_operator, metric).astype(bf16)
    wall_flux = (viscous[None] * wall_grad.astype(f32)).astype(bf16)
    wall_div = wall_derivative(wall_flux, wall_operator, metric)
    wall_part = jnp.sum(strain_wide[None] * wall_grad.astype(f32) ** 2, axis=(0, 1))

    total = stream_div.astype(f32) + wall_div
    total = total + span_div.astype(f32)
    updated = (adjoint.astype(f32) + time_step * total).astype(bf16)

    partial_sum = stream_part + span_part + wall_part
    pieces = partial_sum.reshape(nzl, gxn, ny // gxn).transpose(1, 0, 2)
    pieces = lax.all_to_all(pieces.reshape(gxn, -1), "gx", 0, 0, tiled=True)
    summed = jnp.sum(pieces, axis=0).reshape(nzl, ny // gxn)
    gradient = -summed / nx
    return (updated, gradient)


def solution(mesh):
    in_specs = (P(None, "gx", "gz", None), P("gx", "gz", None), P("gz", None), P(), P(), P(), P())
    out_specs = (P(None, "gx", "gz", None), P("gz", "gx"))
    return jax.shard_map(
        on_device, mesh=mesh, in_specs=in_specs, out_specs=out_specs, check_vma=False
    )
```

```python
import jax
import jax.numpy as jnp
from jax import lax
from jax.sharding import PartitionSpec as P

near_coef = 7.0 / 9.0
far_coef = 1.0 / 36.0
time_step = 0.25
f32 = jnp.float32
bf16 = jnp.bfloat16


def stencil(source, axis):
    widened = source.astype(f32)
    near_diff = jnp.roll(widened, -1, axis) - jnp.roll(widened, 1, axis)
    far_diff = jnp.roll(widened, -2, axis) - jnp.roll(widened, 2, axis)
    return (near_coef * near_diff + far_coef * far_diff).astype(bf16)


def derivative(pencil, operator):
    right_side = stencil(pencil, 1)
    product = jnp.einsum("ij,cjp->cip", operator, right_side, preferred_element_type=f32)
    return product.astype(bf16)


def row_derivative(pencil, operator):
    right_side = stencil(pencil, 0)
    return jnp.dot(operator, right_side, preferred_element_type=f32).astype(bf16)


def wall_derivative(source, wall_operator, metric):
    product = jnp.einsum("kxzj,ij->kxzi", source, wall_operator, preferred_element_type=f32)
    return product * metric


def on_device(adjoint, strain, correction, metric, stream_inverse, span_inverse, wall_operator):
    comps, nxl, nzl, ny = adjoint.shape
    gxn = lax.axis_size("gx")
    lanes = nzl * ny // gxn
    yparts = ny // lanes
    nx = nxl * gxn
    strain_wide = strain.astype(f32)
    viscosity = (correction[None] * strain_wide).astype(bf16)
    viscous = viscosity.astype(f32)

    xs = jnp.concatenate([adjoint, strain[None]], axis=0)
    xs = xs.reshape(comps + 1, nxl, nzl, yparts, lanes).transpose(2, 3, 1, 0, 4)
    xs = xs.reshape(gxn, nxl, (comps + 1) * lanes)
    xt = lax.all_to_all(xs, "gx", 0, 0, tiled=True).reshape(nx, (comps + 1) * lanes)
    stream_strain = xt[:, comps * lanes:].astype(f32)
    me = lax.axis_index("gx")
    z_at, y_at = me // yparts, me % yparts
    corr_row = lax.dynamic_slice(correction, (z_at, y_at * lanes), (1, lanes))
    stream_visc = (corr_row * stream_strain).astype(bf16).astype(f32)
    stream_visc = jnp.tile(stream_visc, (1, comps))
    stream_grad = row_derivative(xt[:, : comps * lanes], stream_inverse)
    stream_flux = (stream_visc * stream_grad.astype(f32)).astype(bf16)
    stream_div = row_derivative(stream_flux, stream_inverse)
    stream_sq = (stream_grad.astype(f32) ** 2).reshape(nx, comps, lanes).sum(axis=1)
    stream_sq = jnp.sum(stream_strain * stream_sq, axis=0)
    back = lax.all_to_all(stream_div.reshape(gxn, nxl, comps * lanes), "gx", 0, 0, tiled=True)
    back = back.reshape(nzl, yparts, nxl, comps, lanes).transpose(3, 2, 0, 1, 4)
    stream_div = back.reshape(comps, nxl, nzl, ny)
    z_ids = lax.broadcasted_iota(jnp.int32, (nzl, yparts, lanes), 0)
    y_ids = lax.broadcasted_iota(jnp.int32, (nzl, yparts, lanes), 1)
    owned = (z_ids == z_at) & (y_ids == y_at)
    stream_part = jnp.where(owned, stream_sq[None, None], 0.0).reshape(nzl, ny)

    zs = jnp.concatenate([adjoint, viscosity[None], strain[None]], axis=0)
    zt = lax.all_to_all(zs, "gz", 1, 2, tiled=True)[:, 0]
    span_visc = zt[comps].astype(f32)
    span_strain = zt[comps + 1].astype(f32)
    span_grad = derivative(zt[:comps], span_inverse)
    span_flux = (span_visc[None] * span_grad.astype(f32)).astype(bf16)
    span_div = derivative(span_flux, span_inverse)
    span_sq = jnp.sum(span_strain[None] * span_grad.astype(f32) ** 2, axis=0)
    span_div = lax.all_to_all(span_div[:, None], "gz", 2, 1, tiled=True)
    span_part = jnp.sum(lax.all_to_all(span_sq[None], "gz", 1, 0, tiled=True), axis=0)

    wall_grad = wall_derivative(adjoint, wall_operator, metric).astype(bf16)
    wall_flux = (viscous[None] * wall_grad.astype(f32)).astype(bf16)
    wall_div = wall_derivative(wall_flux, wall_operator, metric)
    wall_part = jnp.sum(strain_wide[None] * wall_grad.astype(f32) ** 2, axis=(0, 1))

    total = stream_div.astype(f32) + wall_div
    total = total + span_div.astype(f32)
    updated = (adjoint.astype(f32) + time_step * total).astype(bf16)

    partial_sum = stream_part + span_part + wall_part
    pieces = partial_sum.T.reshape(gxn, -1)
    pieces = lax.all_to_all(pieces, "gx", 0, 0, tiled=True)
    summed = jnp.sum(pieces, axis=0).reshape(ny // gxn, nzl).T
    gradient = -summed / nx
    return (updated, gradient)


def solution(mesh):
    in_specs = (P(None, "gx", "gz", None), P("gx", "gz", None), P("gz", None), P(), P(), P(), P())
    out_specs = (P(None, "gx", "gz", None), P("gz", "gx"))
    return jax.shard_map(
        on_device, mesh=mesh, in_specs=in_specs, out_specs=out_specs, check_vma=False
    )
```

```python
import jax
import jax.numpy as jnp
from jax import lax
from jax.sharding import PartitionSpec as P

near_coef = 7.0 / 9.0
far_coef = 1.0 / 36.0
time_step = 0.25
f32 = jnp.float32
bf16 = jnp.bfloat16


def stencil(source, axis):
    widened = source.astype(f32)
    near_diff = jnp.roll(widened, -1, axis) - jnp.roll(widened, 1, axis)
    far_diff = jnp.roll(widened, -2, axis) - jnp.roll(widened, 2, axis)
    return (near_coef * near_diff + far_coef * far_diff).astype(bf16)


def derivative(pencil, operator):
    right_side = stencil(pencil, 1)
    product = jnp.einsum("ij,cjp->cip", operator, right_side, preferred_element_type=f32)
    return product.astype(bf16)


def split_wide(value):
    high = lax.reduce_precision(value, exponent_bits=8, mantissa_bits=7)
    return jnp.stack([high.astype(bf16), (value - high).astype(bf16)])


def join_wide(parts):
    return parts[0].astype(f32) + parts[1].astype(f32)


def row_derivative(pencil, operator):
    right_side = stencil(pencil, 0)
    return jnp.dot(operator, right_side, preferred_element_type=f32).astype(bf16)


def wall_derivative(source, wall_operator, metric):
    product = jnp.einsum("kxzj,ij->kxzi", source, wall_operator, preferred_element_type=f32)
    return product * metric


def on_device(adjoint, strain, correction, metric, stream_inverse, span_inverse, wall_operator):
    comps, nxl, nzl, ny = adjoint.shape
    gxn = lax.axis_size("gx")
    lanes = nzl * ny // gxn
    yparts = ny // lanes
    nx = nxl * gxn
    strain_wide = strain.astype(f32)
    viscosity = (correction[None] * strain_wide).astype(bf16)
    viscous = viscosity.astype(f32)

    xs = jnp.concatenate([adjoint, strain[None]], axis=0)
    xs = xs.reshape(comps + 1, nxl, nzl, yparts, lanes).transpose(2, 3, 1, 0, 4)
    xs = xs.reshape(gxn, nxl, (comps + 1) * lanes)
    xt = lax.all_to_all(xs, "gx", 0, 0, tiled=True).reshape(nx, (comps + 1) * lanes)
    stream_strain = xt[:, comps * lanes:].astype(f32)
    me = lax.axis_index("gx")
    z_at, y_at = me // yparts, me % yparts
    corr_row = lax.dynamic_slice(correction, (z_at, y_at * lanes), (1, lanes))
    stream_visc = (corr_row * stream_strain).astype(bf16).astype(f32)
    stream_visc = jnp.tile(stream_visc, (1, comps))
    stream_grad = row_derivative(xt[:, : comps * lanes], stream_inverse)
    stream_flux = (stream_visc * stream_grad.astype(f32)).astype(bf16)
    stream_div = row_derivative(stream_flux, stream_inverse)
    stream_sq = (stream_grad.astype(f32) ** 2).reshape(nx, comps, lanes).sum(axis=1)
    stream_sq = jnp.sum(stream_strain * stream_sq, axis=0)
    z_ids = lax.broadcasted_iota(jnp.int32, (nzl, yparts, lanes), 0)
    y_ids = lax.broadcasted_iota(jnp.int32, (nzl, yparts, lanes), 1)
    owned = (z_ids == z_at) & (y_ids == y_at)
    stream_part = jnp.where(owned, stream_sq[None, None], 0.0).reshape(nzl, ny)

    zs = jnp.concatenate([adjoint, viscosity[None], strain[None]], axis=0)
    zt = lax.all_to_all(zs, "gz", 1, 2, tiled=True)[:, 0]
    span_visc = zt[comps].astype(f32)
    span_strain = zt[comps + 1].astype(f32)
    span_grad = derivative(zt[:comps], span_inverse)
    span_flux = (span_visc[None] * span_grad.astype(f32)).astype(bf16)
    span_div = derivative(span_flux, span_inverse)
    span_sq = jnp.sum(span_strain[None] * span_grad.astype(f32) ** 2, axis=0)
    span_back = jnp.concatenate([span_div, split_wide(span_sq)], axis=0)
    span_back = lax.all_to_all(span_back[:, None], "gz", 2, 1, tiled=True)
    span_div = span_back[:comps]
    span_part = jnp.sum(join_wide(span_back[comps:]), axis=0)

    wall_grad = wall_derivative(adjoint, wall_operator, metric).astype(bf16)
    wall_flux = (viscous[None] * wall_grad.astype(f32)).astype(bf16)
    wall_div = wall_derivative(wall_flux, wall_operator, metric)
    wall_part = jnp.sum(strain_wide[None] * wall_grad.astype(f32) ** 2, axis=(0, 1))

    partial_sum = stream_part + span_part + wall_part
    pieces = split_wide(partial_sum.T.reshape(gxn, -1))
    extra = jnp.zeros((gxn, nxl - 2, lanes), bf16)
    extra = jnp.concatenate([pieces[0][:, None], pieces[1][:, None], extra], axis=1)
    back = jnp.concatenate([stream_div.reshape(gxn, nxl, comps * lanes), extra], axis=2)
    back = lax.all_to_all(back, "gx", 0, 0, tiled=True)
    summed = jnp.sum(join_wide(back[:, :2, comps * lanes:].transpose(1, 0, 2)), axis=0)
    summed = summed.reshape(ny // gxn, nzl).T
    back = back[:, :, : comps * lanes].reshape(nzl, yparts, nxl, comps, lanes)
    stream_div = back.transpose(3, 2, 0, 1, 4).reshape(comps, nxl, nzl, ny)

    total = stream_div.astype(f32) + wall_div
    total = total + span_div.astype(f32)
    updated = (adjoint.astype(f32) + time_step * total).astype(bf16)

    gradient = -summed / nx
    return (updated, gradient)


def solution(mesh):
    in_specs = (P(None, "gx", "gz", None), P("gx", "gz", None), P("gz", None), P(), P(), P(), P())
    out_specs = (P(None, "gx", "gz", None), P("gz", "gx"))
    return jax.shard_map(
        on_device, mesh=mesh, in_specs=in_specs, out_specs=out_specs, check_vma=False
    )
```

```python
import jax
import jax.numpy as jnp
from jax import lax
from jax.sharding import PartitionSpec as P

near_coef = 7.0 / 9.0
far_coef = 1.0 / 36.0
time_step = 0.25
f32 = jnp.float32
bf16 = jnp.bfloat16


def stencil(source, axis):
    widened = source.astype(f32)
    near_diff = jnp.roll(widened, -1, axis) - jnp.roll(widened, 1, axis)
    far_diff = jnp.roll(widened, -2, axis) - jnp.roll(widened, 2, axis)
    return (near_coef * near_diff + far_coef * far_diff).astype(bf16)


def derivative(pencil, operator):
    right_side = stencil(pencil, 1)
    product = jnp.einsum("ij,cjp->cip", operator, right_side, preferred_element_type=f32)
    return product.astype(bf16)


def exchange(block_for, size, mine):
    received = [block_for(mine)]
    for shift in range(1, size):
        pairs = [(src, (src + shift) % size) for src in range(size)]
        received.append(lax.ppermute(block_for((mine + shift) % size), "gz", pairs))
    return jnp.stack(received)


def in_order(received, size, mine):
    flipped = jnp.concatenate([received[:1], received[1:][::-1]], axis=0)
    doubled = jnp.concatenate([flipped, flipped], axis=0)
    return lax.dynamic_slice_in_dim(doubled, size - mine, size, 0)


def split_wide(value):
    high = lax.reduce_precision(value, exponent_bits=8, mantissa_bits=7)
    return jnp.stack([high.astype(bf16), (value - high).astype(bf16)])


def join_wide(parts):
    return parts[0].astype(f32) + parts[1].astype(f32)


def row_derivative(pencil, operator):
    right_side = stencil(pencil, 0)
    return jnp.dot(operator, right_side, preferred_element_type=f32).astype(bf16)


def wall_derivative(source, wall_operator, metric):
    product = jnp.einsum("kxzj,ij->kxzi", source, wall_operator, preferred_element_type=f32)
    return product * metric


def on_device(adjoint, strain, correction, metric, stream_inverse, span_inverse, wall_operator):
    comps, nxl, nzl, ny = adjoint.shape
    gxn = lax.axis_size("gx")
    lanes = nzl * ny // gxn
    yparts = ny // lanes
    nx = nxl * gxn
    strain_wide = strain.astype(f32)
    viscosity = (correction[None] * strain_wide).astype(bf16)
    viscous = viscosity.astype(f32)

    xs = jnp.concatenate([adjoint, strain[None]], axis=0)
    xs = xs.reshape(comps + 1, nxl, nzl, yparts, lanes).transpose(2, 3, 1, 0, 4)
    xs = xs.reshape(gxn, nxl, (comps + 1) * lanes)
    xt = lax.all_to_all(xs, "gx", 0, 0, tiled=True).reshape(nx, (comps + 1) * lanes)
    stream_strain = xt[:, comps * lanes:].astype(f32)
    me = lax.axis_index("gx")
    z_at, y_at = me // yparts, me % yparts
    corr_row = lax.dynamic_slice(correction, (z_at, y_at * lanes), (1, lanes))
    stream_visc = (corr_row * stream_strain).astype(bf16).astype(f32)
    stream_visc = jnp.tile(stream_visc, (1, comps))
    stream_grad = row_derivative(xt[:, : comps * lanes], stream_inverse)
    stream_flux = (stream_visc * stream_grad.astype(f32)).astype(bf16)
    stream_div = row_derivative(stream_flux, stream_inverse)
    stream_sq = (stream_grad.astype(f32) ** 2).reshape(nx, comps, lanes).sum(axis=1)
    stream_sq = jnp.sum(stream_strain * stream_sq, axis=0)
    z_ids = lax.broadcasted_iota(jnp.int32, (nzl, yparts, lanes), 0)
    y_ids = lax.broadcasted_iota(jnp.int32, (nzl, yparts, lanes), 1)
    owned = (z_ids == z_at) & (y_ids == y_at)
    stream_part = jnp.where(owned, stream_sq[None, None], 0.0).reshape(nzl, ny)

    gzn = lax.axis_size("gz")
    mine = lax.axis_index("gz")
    zs = jnp.concatenate([adjoint, viscosity[None], strain[None]], axis=0)
    span_in = exchange(lambda dst: lax.dynamic_index_in_dim(zs, dst, 1, False), gzn, mine)
    zt = in_order(span_in, gzn, mine)
    zt = zt.transpose(1, 0, 2, 3).reshape(zs.shape[0], gzn * nzl, ny)
    span_visc = zt[comps].astype(f32)
    span_strain = zt[comps + 1].astype(f32)
    span_grad = derivative(zt[:comps], span_inverse)
    span_flux = (span_visc[None] * span_grad.astype(f32)).astype(bf16)
    span_div = derivative(span_flux, span_inverse)
    span_sq = jnp.sum(span_strain[None] * span_grad.astype(f32) ** 2, axis=0)
    span_back = jnp.concatenate([span_div, split_wide(span_sq)], axis=0)
    span_out = exchange(
        lambda dst: lax.dynamic_slice_in_dim(span_back, dst * nzl, nzl, 1), gzn, mine
    )
    span_part = jnp.sum(join_wide(span_out[:, comps:].transpose(1, 0, 2, 3)), axis=0)
    span_div = in_order(span_out[:, :comps], gzn, mine).transpose(1, 0, 2, 3)

    wall_grad = wall_derivative(adjoint, wall_operator, metric).astype(bf16)
    wall_flux = (viscous[None] * wall_grad.astype(f32)).astype(bf16)
    wall_div = wall_derivative(wall_flux, wall_operator, metric)
    wall_part = jnp.sum(strain_wide[None] * wall_grad.astype(f32) ** 2, axis=(0, 1))

    partial_sum = stream_part + span_part + wall_part
    pieces = split_wide(partial_sum.T.reshape(gxn, -1))
    extra = jnp.zeros((gxn, nxl - 2, lanes), bf16)
    extra = jnp.concatenate([pieces[0][:, None], pieces[1][:, None], extra], axis=1)
    back = jnp.concatenate([stream_div.reshape(gxn, nxl, comps * lanes), extra], axis=2)
    back = lax.all_to_all(back, "gx", 0, 0, tiled=True)
    summed = jnp.sum(join_wide(back[:, :2, comps * lanes:].transpose(1, 0, 2)), axis=0)
    summed = summed.reshape(ny // gxn, nzl).T
    back = back[:, :, : comps * lanes].reshape(nzl, yparts, nxl, comps, lanes)
    stream_div = back.transpose(3, 2, 0, 1, 4).reshape(comps, nxl, nzl, ny)

    total = stream_div.astype(f32) + wall_div
    total = total + span_div.astype(f32)
    updated = (adjoint.astype(f32) + time_step * total).astype(bf16)

    gradient = -summed / nx
    return (updated, gradient)


def solution(mesh):
    in_specs = (P(None, "gx", "gz", None), P("gx", "gz", None), P("gz", None), P(), P(), P(), P())
    out_specs = (P(None, "gx", "gz", None), P("gz", "gx"))
    return jax.shard_map(
        on_device, mesh=mesh, in_specs=in_specs, out_specs=out_specs, check_vma=False
    )
```

```python
import jax
import jax.numpy as jnp
from jax import lax
from jax.sharding import PartitionSpec as P

near_coef = 7.0 / 9.0
far_coef = 1.0 / 36.0
time_step = 0.25
f32 = jnp.float32
bf16 = jnp.bfloat16


def stencil(source, axis):
    widened = source.astype(f32)
    near_diff = jnp.roll(widened, -1, axis) - jnp.roll(widened, 1, axis)
    far_diff = jnp.roll(widened, -2, axis) - jnp.roll(widened, 2, axis)
    return (near_coef * near_diff + far_coef * far_diff).astype(bf16)


def derivative(pencil, operator):
    right_side = stencil(pencil, 1)
    product = jnp.einsum("ij,cjp->cip", operator, right_side, preferred_element_type=f32)
    return product.astype(bf16)


def xor_order(blocks, mine):
    size = blocks.shape[0]
    bit = 1
    while bit < size:
        swapped = blocks.reshape(size // (2 * bit), 2, bit, *blocks.shape[1:])[:, ::-1]
        blocks = jnp.where((mine // bit) % 2 == 1, swapped.reshape(blocks.shape), blocks)
        bit *= 2
    return blocks


def butterfly(blocks, mine):
    size = blocks.shape[0]
    blocks = xor_order(blocks, mine)
    bit = 1
    while bit < size:
        split = blocks.reshape(size // (2 * bit), 2, bit, *blocks.shape[1:])
        pairs = [(src, src ^ bit) for src in range(size)]
        moved = lax.ppermute(split[:, 1], "gz", pairs)
        blocks = jnp.stack([split[:, 0], moved], axis=1).reshape(blocks.shape)
        bit *= 2
    return xor_order(blocks, mine)


def split_wide(value):
    high = lax.reduce_precision(value, exponent_bits=8, mantissa_bits=7)
    return jnp.stack([high.astype(bf16), (value - high).astype(bf16)])


def join_wide(parts):
    return parts[0].astype(f32) + parts[1].astype(f32)


def row_derivative(pencil, operator):
    right_side = stencil(pencil, 0)
    return jnp.dot(operator, right_side, preferred_element_type=f32).astype(bf16)


def wall_derivative(source, wall_operator, metric):
    product = jnp.einsum("kxzj,ij->kxzi", source, wall_operator, preferred_element_type=f32)
    return product * metric


def on_device(adjoint, strain, correction, metric, stream_inverse, span_inverse, wall_operator):
    comps, nxl, nzl, ny = adjoint.shape
    gxn = lax.axis_size("gx")
    lanes = nzl * ny // gxn
    yparts = ny // lanes
    nx = nxl * gxn
    strain_wide = strain.astype(f32)
    viscosity = (correction[None] * strain_wide).astype(bf16)
    viscous = viscosity.astype(f32)

    xs = jnp.concatenate([adjoint, strain[None]], axis=0)
    xs = xs.reshape(comps + 1, nxl, nzl, yparts, lanes).transpose(2, 3, 1, 0, 4)
    xs = xs.reshape(gxn, nxl, (comps + 1) * lanes)
    xt = lax.all_to_all(xs, "gx", 0, 0, tiled=True).reshape(nx, (comps + 1) * lanes)
    stream_strain = xt[:, comps * lanes:].astype(f32)
    me = lax.axis_index("gx")
    z_at, y_at = me // yparts, me % yparts
    corr_row = lax.dynamic_slice(correction, (z_at, y_at * lanes), (1, lanes))
    stream_visc = (corr_row * stream_strain).astype(bf16).astype(f32)
    stream_visc = jnp.tile(stream_visc, (1, comps))
    stream_grad = row_derivative(xt[:, : comps * lanes], stream_inverse)
    stream_flux = (stream_visc * stream_grad.astype(f32)).astype(bf16)
    stream_div = row_derivative(stream_flux, stream_inverse)
    stream_sq = (stream_grad.astype(f32) ** 2).reshape(nx, comps, lanes).sum(axis=1)
    stream_sq = jnp.sum(stream_strain * stream_sq, axis=0)
    z_ids = lax.broadcasted_iota(jnp.int32, (nzl, yparts, lanes), 0)
    y_ids = lax.broadcasted_iota(jnp.int32, (nzl, yparts, lanes), 1)
    owned = (z_ids == z_at) & (y_ids == y_at)
    stream_part = jnp.where(owned, stream_sq[None, None], 0.0).reshape(nzl, ny)

    gzn = lax.axis_size("gz")
    mine = lax.axis_index("gz")
    zs = jnp.concatenate([adjoint, viscosity[None], strain[None]], axis=0)
    zt = butterfly(zs.transpose(1, 0, 2, 3), mine)
    zt = zt.transpose(1, 0, 2, 3).reshape(zs.shape[0], gzn * nzl, ny)
    span_visc = zt[comps].astype(f32)
    span_strain = zt[comps + 1].astype(f32)
    span_grad = derivative(zt[:comps], span_inverse)
    span_flux = (span_visc[None] * span_grad.astype(f32)).astype(bf16)
    span_div = derivative(span_flux, span_inverse)
    span_sq = jnp.sum(span_strain[None] * span_grad.astype(f32) ** 2, axis=0)
    span_back = jnp.concatenate([span_div, split_wide(span_sq)], axis=0)
    span_back = span_back.reshape(span_back.shape[0], gzn, nzl, ny).transpose(1, 0, 2, 3)
    span_out = butterfly(span_back, mine)
    span_part = jnp.sum(join_wide(span_out[:, comps:].transpose(1, 0, 2, 3)), axis=0)
    span_div = span_out[:, :comps].transpose(1, 0, 2, 3)

    wall_grad = wall_derivative(adjoint, wall_operator, metric).astype(bf16)
    wall_flux = (viscous[None] * wall_grad.astype(f32)).astype(bf16)
    wall_div = wall_derivative(wall_flux, wall_operator, metric)
    wall_part = jnp.sum(strain_wide[None] * wall_grad.astype(f32) ** 2, axis=(0, 1))

    partial_sum = stream_part + span_part + wall_part
    pieces = split_wide(partial_sum.T.reshape(gxn, -1))
    extra = jnp.zeros((gxn, nxl - 2, lanes), bf16)
    extra = jnp.concatenate([pieces[0][:, None], pieces[1][:, None], extra], axis=1)
    back = jnp.concatenate([stream_div.reshape(gxn, nxl, comps * lanes), extra], axis=2)
    back = lax.all_to_all(back, "gx", 0, 0, tiled=True)
    summed = jnp.sum(join_wide(back[:, :2, comps * lanes:].transpose(1, 0, 2)), axis=0)
    summed = summed.reshape(ny // gxn, nzl).T
    back = back[:, :, : comps * lanes].reshape(nzl, yparts, nxl, comps, lanes)
    stream_div = back.transpose(3, 2, 0, 1, 4).reshape(comps, nxl, nzl, ny)

    total = stream_div.astype(f32) + wall_div
    total = total + span_div.astype(f32)
    updated = (adjoint.astype(f32) + time_step * total).astype(bf16)

    gradient = -summed / nx
    return (updated, gradient)


def solution(mesh):
    in_specs = (P(None, "gx", "gz", None), P("gx", "gz", None), P("gz", None), P(), P(), P(), P())
    out_specs = (P(None, "gx", "gz", None), P("gz", "gx"))
    return jax.shard_map(
        on_device, mesh=mesh, in_specs=in_specs, out_specs=out_specs, check_vma=False
    )
```

```python
import jax
import jax.numpy as jnp
from jax import lax
from jax.sharding import PartitionSpec as P

near_coef = 7.0 / 9.0
far_coef = 1.0 / 36.0
time_step = 0.25
f32 = jnp.float32
bf16 = jnp.bfloat16


def stencil(source, axis):
    widened = source.astype(f32)
    near_diff = jnp.roll(widened, -1, axis) - jnp.roll(widened, 1, axis)
    far_diff = jnp.roll(widened, -2, axis) - jnp.roll(widened, 2, axis)
    return (near_coef * near_diff + far_coef * far_diff).astype(bf16)


def derivative(pencil, operator):
    right_side = stencil(pencil, 1)
    product = jnp.einsum("ij,cjp->cip", operator, right_side, preferred_element_type=f32)
    return product.astype(bf16)


def xor_order(blocks, mine):
    size = blocks.shape[0]
    bit = 1
    while bit < size:
        swapped = blocks.reshape(size // (2 * bit), 2, bit, *blocks.shape[1:])[:, ::-1]
        blocks = jnp.where((mine // bit) % 2 == 1, swapped.reshape(blocks.shape), blocks)
        bit *= 2
    return blocks


def butterfly(blocks, mine):
    size = blocks.shape[0]
    blocks = xor_order(blocks, mine)
    bit = 1
    while bit < size:
        split = blocks.reshape(size // (2 * bit), 2, bit, *blocks.shape[1:])
        pairs = [(src, src ^ bit) for src in range(size)]
        moved = lax.ppermute(split[:, 1], "gz", pairs)
        blocks = jnp.stack([split[:, 0], moved], axis=1).reshape(blocks.shape)
        bit *= 2
    return xor_order(blocks, mine)


def split_wide(value):
    high = lax.reduce_precision(value, exponent_bits=8, mantissa_bits=7)
    return jnp.stack([high.astype(bf16), (value - high).astype(bf16)])


def join_wide(parts):
    return parts[0].astype(f32) + parts[1].astype(f32)


def row_derivative(pencil, operator):
    right_side = stencil(pencil, 0)
    return jnp.dot(operator, right_side, preferred_element_type=f32).astype(bf16)


def wall_derivative(source, wall_operator, metric):
    product = jnp.einsum("kxzj,ij->kxzi", source, wall_operator, preferred_element_type=f32)
    return product * metric


def on_device(adjoint, strain, correction, metric, stream_inverse, span_inverse, wall_operator):
    comps, nxl, nzl, ny = adjoint.shape
    gxn = lax.axis_size("gx")
    lanes = nzl * ny // gxn
    yparts = ny // lanes
    nx = nxl * gxn
    strain_wide = strain.astype(f32)
    viscosity = (correction[None] * strain_wide).astype(bf16)
    viscous = viscosity.astype(f32)

    xs = jnp.concatenate([adjoint, strain[None]], axis=0)
    xs = xs.reshape(comps + 1, nxl, nzl, yparts, lanes).transpose(2, 3, 1, 0, 4)
    xs = xs.reshape(gxn, nxl, (comps + 1) * lanes)
    xt = lax.all_to_all(xs, "gx", 0, 0, tiled=True).reshape(nx, (comps + 1) * lanes)
    stream_strain = xt[:, comps * lanes:].astype(f32)
    me = lax.axis_index("gx")
    z_at, y_at = me // yparts, me % yparts
    corr_row = lax.dynamic_slice(correction, (z_at, y_at * lanes), (1, lanes))
    stream_visc = (corr_row * stream_strain).astype(bf16).astype(f32)
    stream_visc = jnp.tile(stream_visc, (1, comps))
    stream_grad = row_derivative(xt[:, : comps * lanes], stream_inverse)
    stream_flux = (stream_visc * stream_grad.astype(f32)).astype(bf16)
    stream_div = row_derivative(stream_flux, stream_inverse)
    stream_sq = (stream_grad.astype(f32) ** 2).reshape(nx, comps, lanes).sum(axis=1)
    stream_sq = jnp.sum(stream_strain * stream_sq, axis=0)
    z_ids = lax.broadcasted_iota(jnp.int32, (nzl, yparts, lanes), 0)
    y_ids = lax.broadcasted_iota(jnp.int32, (nzl, yparts, lanes), 1)
    owned = (z_ids == z_at) & (y_ids == y_at)
    stream_part = jnp.where(owned, stream_sq[None, None], 0.0).reshape(nzl, ny)

    gzn = lax.axis_size("gz")
    mine = lax.axis_index("gz")
    zs = jnp.concatenate([adjoint, viscosity[None], strain[None]], axis=0)
    zt = lax.all_to_all(zs, "gz", 1, 2, tiled=True)[:, 0]
    span_visc = zt[comps].astype(f32)
    span_strain = zt[comps + 1].astype(f32)
    span_grad = derivative(zt[:comps], span_inverse)
    span_flux = (span_visc[None] * span_grad.astype(f32)).astype(bf16)
    span_div = derivative(span_flux, span_inverse)
    span_sq = jnp.sum(span_strain[None] * span_grad.astype(f32) ** 2, axis=0)
    span_back = jnp.concatenate([span_div, split_wide(span_sq)], axis=0)
    span_back = span_back.reshape(span_back.shape[0], gzn, nzl, ny).transpose(1, 0, 2, 3)
    span_out = butterfly(span_back, mine)
    span_part = jnp.sum(join_wide(span_out[:, comps:].transpose(1, 0, 2, 3)), axis=0)
    span_div = span_out[:, :comps].transpose(1, 0, 2, 3)

    wall_grad = wall_derivative(adjoint, wall_operator, metric).astype(bf16)
    wall_flux = (viscous[None] * wall_grad.astype(f32)).astype(bf16)
    wall_div = wall_derivative(wall_flux, wall_operator, metric)
    wall_part = jnp.sum(strain_wide[None] * wall_grad.astype(f32) ** 2, axis=(0, 1))

    partial_sum = stream_part + span_part + wall_part
    pieces = split_wide(partial_sum.T.reshape(gxn, -1))
    extra = jnp.zeros((gxn, nxl - 2, lanes), bf16)
    extra = jnp.concatenate([pieces[0][:, None], pieces[1][:, None], extra], axis=1)
    back = jnp.concatenate([stream_div.reshape(gxn, nxl, comps * lanes), extra], axis=2)
    back = lax.all_to_all(back, "gx", 0, 0, tiled=True)
    summed = jnp.sum(join_wide(back[:, :2, comps * lanes:].transpose(1, 0, 2)), axis=0)
    summed = summed.reshape(ny // gxn, nzl).T
    back = back[:, :, : comps * lanes].reshape(nzl, yparts, nxl, comps, lanes)
    stream_div = back.transpose(3, 2, 0, 1, 4).reshape(comps, nxl, nzl, ny)

    total = stream_div.astype(f32) + wall_div
    total = total + span_div.astype(f32)
    updated = (adjoint.astype(f32) + time_step * total).astype(bf16)

    gradient = -summed / nx
    return (updated, gradient)


def solution(mesh):
    in_specs = (P(None, "gx", "gz", None), P("gx", "gz", None), P("gz", None), P(), P(), P(), P())
    out_specs = (P(None, "gx", "gz", None), P("gz", "gx"))
    return jax.shard_map(
        on_device, mesh=mesh, in_specs=in_specs, out_specs=out_specs, check_vma=False
    )
```

```python
import jax
import jax.numpy as jnp
from jax import lax
from jax.sharding import PartitionSpec as P

near_coef = 7.0 / 9.0
far_coef = 1.0 / 36.0
time_step = 0.25
f32 = jnp.float32
bf16 = jnp.bfloat16


def folded(operator):
    wide = operator.astype(f32)
    shifted = lambda step: jnp.roll(wide, step, 1)
    merged = near_coef * (shifted(1) - shifted(-1)) + far_coef * (shifted(2) - shifted(-2))
    return split_wide(merged)


def derivative(pencil, operator):
    product = sum(
        jnp.einsum("ij,cjp->cip", part, pencil, preferred_element_type=f32) for part in operator
    )
    return product.astype(bf16)


def xor_order(blocks, mine):
    size = blocks.shape[0]
    bit = 1
    while bit < size:
        swapped = blocks.reshape(size // (2 * bit), 2, bit, *blocks.shape[1:])[:, ::-1]
        blocks = jnp.where((mine // bit) % 2 == 1, swapped.reshape(blocks.shape), blocks)
        bit *= 2
    return blocks


def butterfly(blocks, mine):
    size = blocks.shape[0]
    blocks = xor_order(blocks, mine)
    bit = 1
    while bit < size:
        split = blocks.reshape(size // (2 * bit), 2, bit, *blocks.shape[1:])
        pairs = [(src, src ^ bit) for src in range(size)]
        moved = lax.ppermute(split[:, 1], "gz", pairs)
        blocks = jnp.stack([split[:, 0], moved], axis=1).reshape(blocks.shape)
        bit *= 2
    return xor_order(blocks, mine)


def split_wide(value):
    high = lax.reduce_precision(value, exponent_bits=8, mantissa_bits=7)
    return jnp.stack([high.astype(bf16), (value - high).astype(bf16)])


def join_wide(parts):
    return parts[0].astype(f32) + parts[1].astype(f32)


def row_derivative(pencil, operator):
    product = sum(jnp.dot(part, pencil, preferred_element_type=f32) for part in operator)
    return product.astype(bf16)


def wall_derivative(source, wall_operator, metric):
    product = jnp.einsum("kxzj,ij->kxzi", source, wall_operator, preferred_element_type=f32)
    return product * metric


def on_device(adjoint, strain, correction, metric, stream_inverse, span_inverse, wall_operator):
    comps, nxl, nzl, ny = adjoint.shape
    gxn = lax.axis_size("gx")
    lanes = nzl * ny // gxn
    yparts = ny // lanes
    nx = nxl * gxn
    stream_inverse = folded(stream_inverse)
    span_inverse = folded(span_inverse)
    strain_wide = strain.astype(f32)
    viscosity = (correction[None] * strain_wide).astype(bf16)
    viscous = viscosity.astype(f32)

    xs = jnp.concatenate([adjoint, strain[None]], axis=0)
    xs = xs.reshape(comps + 1, nxl, nzl, yparts, lanes).transpose(2, 3, 1, 0, 4)
    xs = xs.reshape(gxn, nxl, (comps + 1) * lanes)
    xt = lax.all_to_all(xs, "gx", 0, 0, tiled=True).reshape(nx, (comps + 1) * lanes)
    stream_strain = xt[:, comps * lanes:].astype(f32)
    me = lax.axis_index("gx")
    z_at, y_at = me // yparts, me % yparts
    corr_row = lax.dynamic_slice(correction, (z_at, y_at * lanes), (1, lanes))
    stream_visc = (corr_row * stream_strain).astype(bf16).astype(f32)
    stream_visc = jnp.tile(stream_visc, (1, comps))
    stream_grad = row_derivative(xt[:, : comps * lanes], stream_inverse)
    stream_flux = (stream_visc * stream_grad.astype(f32)).astype(bf16)
    stream_div = row_derivative(stream_flux, stream_inverse)
    stream_sq = (stream_grad.astype(f32) ** 2).reshape(nx, comps, lanes).sum(axis=1)
    stream_sq = jnp.sum(stream_strain * stream_sq, axis=0)
    z_ids = lax.broadcasted_iota(jnp.int32, (nzl, yparts, lanes), 0)
    y_ids = lax.broadcasted_iota(jnp.int32, (nzl, yparts, lanes), 1)
    owned = (z_ids == z_at) & (y_ids == y_at)
    stream_part = jnp.where(owned, stream_sq[None, None], 0.0).reshape(nzl, ny)

    gzn = lax.axis_size("gz")
    mine = lax.axis_index("gz")
    zs = jnp.concatenate([adjoint, viscosity[None], strain[None]], axis=0)
    zt = lax.all_to_all(zs, "gz", 1, 2, tiled=True)[:, 0]
    span_visc = zt[comps].astype(f32)
    span_strain = zt[comps + 1].astype(f32)
    span_grad = derivative(zt[:comps], span_inverse)
    span_flux = (span_visc[None] * span_grad.astype(f32)).astype(bf16)
    span_div = derivative(span_flux, span_inverse)
    span_sq = jnp.sum(span_strain[None] * span_grad.astype(f32) ** 2, axis=0)
    span_back = jnp.concatenate([span_div, split_wide(span_sq)], axis=0)
    span_back = span_back.reshape(span_back.shape[0], gzn, nzl, ny).transpose(1, 0, 2, 3)
    span_out = butterfly(span_back, mine)
    span_part = jnp.sum(join_wide(span_out[:, comps:].transpose(1, 0, 2, 3)), axis=0)
    span_div = span_out[:, :comps].transpose(1, 0, 2, 3)

    wall_grad = wall_derivative(adjoint, wall_operator, metric).astype(bf16)
    wall_flux = (viscous[None] * wall_grad.astype(f32)).astype(bf16)
    wall_div = wall_derivative(wall_flux, wall_operator, metric)
    wall_part = jnp.sum(strain_wide[None] * wall_grad.astype(f32) ** 2, axis=(0, 1))

    partial_sum = stream_part + span_part + wall_part
    pieces = split_wide(partial_sum.T.reshape(gxn, -1))
    extra = jnp.zeros((gxn, nxl - 2, lanes), bf16)
    extra = jnp.concatenate([pieces[0][:, None], pieces[1][:, None], extra], axis=1)
    back = jnp.concatenate([stream_div.reshape(gxn, nxl, comps * lanes), extra], axis=2)
    back = lax.all_to_all(back, "gx", 0, 0, tiled=True)
    summed = jnp.sum(join_wide(back[:, :2, comps * lanes:].transpose(1, 0, 2)), axis=0)
    summed = summed.reshape(ny // gxn, nzl).T
    back = back[:, :, : comps * lanes].reshape(nzl, yparts, nxl, comps, lanes)
    stream_div = back.transpose(3, 2, 0, 1, 4).reshape(comps, nxl, nzl, ny)

    total = stream_div.astype(f32) + wall_div
    total = total + span_div.astype(f32)
    updated = (adjoint.astype(f32) + time_step * total).astype(bf16)

    gradient = -summed / nx
    return (updated, gradient)


def solution(mesh):
    in_specs = (P(None, "gx", "gz", None), P("gx", "gz", None), P("gz", None), P(), P(), P(), P())
    out_specs = (P(None, "gx", "gz", None), P("gz", "gx"))
    return jax.shard_map(
        on_device, mesh=mesh, in_specs=in_specs, out_specs=out_specs, check_vma=False
    )
```

```python
import jax
import jax.numpy as jnp
from jax import lax
from jax.sharding import PartitionSpec as P

near_coef = 7.0 / 9.0
far_coef = 1.0 / 36.0
time_step = 0.25
f32 = jnp.float32
bf16 = jnp.bfloat16


def folded(operator):
    wide = operator.astype(f32)
    shifted = lambda step: jnp.roll(wide, step, 1)
    merged = near_coef * (shifted(1) - shifted(-1)) + far_coef * (shifted(2) - shifted(-2))
    return split_wide(merged)


def stencil(source, axis):
    widened = source.astype(f32)
    near_diff = jnp.roll(widened, -1, axis) - jnp.roll(widened, 1, axis)
    far_diff = jnp.roll(widened, -2, axis) - jnp.roll(widened, 2, axis)
    return (near_coef * near_diff + far_coef * far_diff).astype(bf16)


def derivative(pencil, operator):
    right_side = stencil(pencil, 1)
    product = jnp.einsum("ij,cjp->cip", operator, right_side, preferred_element_type=f32)
    return product.astype(bf16)


def xor_order(blocks, mine):
    size = blocks.shape[0]
    bit = 1
    while bit < size:
        swapped = blocks.reshape(size // (2 * bit), 2, bit, *blocks.shape[1:])[:, ::-1]
        blocks = jnp.where((mine // bit) % 2 == 1, swapped.reshape(blocks.shape), blocks)
        bit *= 2
    return blocks


def butterfly(blocks, mine):
    size = blocks.shape[0]
    blocks = xor_order(blocks, mine)
    bit = 1
    while bit < size:
        split = blocks.reshape(size // (2 * bit), 2, bit, *blocks.shape[1:])
        pairs = [(src, src ^ bit) for src in range(size)]
        moved = lax.ppermute(split[:, 1], "gz", pairs)
        blocks = jnp.stack([split[:, 0], moved], axis=1).reshape(blocks.shape)
        bit *= 2
    return xor_order(blocks, mine)


def split_wide(value):
    high = lax.reduce_precision(value, exponent_bits=8, mantissa_bits=7)
    return jnp.stack([high.astype(bf16), (value - high).astype(bf16)])


def join_wide(parts):
    return parts[0].astype(f32) + parts[1].astype(f32)


def row_derivative(pencil, operator):
    product = sum(jnp.dot(part, pencil, preferred_element_type=f32) for part in operator)
    return product.astype(bf16)


def wall_derivative(source, wall_operator, metric):
    product = jnp.einsum("kxzj,ij->kxzi", source, wall_operator, preferred_element_type=f32)
    return product * metric


def section(adjoint, strain, correction, metric, stream_inverse, span_inverse, wall_operator):
    comps, nxl, nzl, ny = adjoint.shape
    gxn = lax.axis_size("gx")
    lanes = nzl * ny // gxn
    yparts = ny // lanes
    nx = nxl * gxn
    stream_inverse = folded(stream_inverse)
    strain_wide = strain.astype(f32)
    viscosity = (correction[None] * strain_wide).astype(bf16)
    viscous = viscosity.astype(f32)

    xs = jnp.concatenate([adjoint, strain[None]], axis=0)
    xs = xs.reshape(comps + 1, nxl, nzl, yparts, lanes).transpose(2, 3, 1, 0, 4)
    xs = xs.reshape(gxn, nxl, (comps + 1) * lanes)
    xt = lax.all_to_all(xs, "gx", 0, 0, tiled=True)
    xt = xt.reshape(nx, (comps + 1) * lanes)
    stream_strain = xt[:, comps * lanes:].astype(f32)
    me = lax.axis_index("gx")
    z_at, y_at = me // yparts, me % yparts
    corr_row = lax.dynamic_slice(correction, (z_at, y_at * lanes), (1, lanes))
    stream_visc = (corr_row * stream_strain).astype(bf16).astype(f32)
    stream_visc = jnp.tile(stream_visc, (1, comps))
    stream_grad = row_derivative(xt[:, : comps * lanes], stream_inverse)
    stream_flux = (stream_visc * stream_grad.astype(f32)).astype(bf16)
    stream_div = row_derivative(stream_flux, stream_inverse)
    stream_sq = (stream_grad.astype(f32) ** 2).reshape(nx, comps, lanes).sum(axis=1)
    stream_sq = jnp.sum(stream_strain * stream_sq, axis=0)
    z_ids = lax.broadcasted_iota(jnp.int32, (nzl, yparts, lanes), 0)
    y_ids = lax.broadcasted_iota(jnp.int32, (nzl, yparts, lanes), 1)
    owned = (z_ids == z_at) & (y_ids == y_at)
    stream_part = jnp.where(owned, stream_sq[None, None], 0.0).reshape(nzl, ny)

    gzn = lax.axis_size("gz")
    mine = lax.axis_index("gz")
    zs = jnp.concatenate([adjoint, viscosity[None], strain[None]], axis=0)
    zt = lax.all_to_all(zs, "gz", 1, 2, tiled=True)[:, 0]
    span_visc = zt[comps].astype(f32)
    span_strain = zt[comps + 1].astype(f32)
    span_grad = derivative(zt[:comps], span_inverse)
    span_flux = (span_visc[None] * span_grad.astype(f32)).astype(bf16)
    span_div = derivative(span_flux, span_inverse)
    span_sq = jnp.sum(span_strain[None] * span_grad.astype(f32) ** 2, axis=0)
    span_back = jnp.concatenate([span_div, split_wide(span_sq)], axis=0)
    span_back = span_back.reshape(span_back.shape[0], gzn, nzl, ny).transpose(1, 0, 2, 3)
    span_out = butterfly(span_back, mine)
    span_part = jnp.sum(join_wide(span_out[:, comps:].transpose(1, 0, 2, 3)), axis=0)
    span_div = span_out[:, :comps].transpose(1, 0, 2, 3)

    wall_grad = wall_derivative(adjoint, wall_operator, metric).astype(bf16)
    wall_flux = (viscous[None] * wall_grad.astype(f32)).astype(bf16)
    wall_div = wall_derivative(wall_flux, wall_operator, metric)
    wall_part = jnp.sum(strain_wide[None] * wall_grad.astype(f32) ** 2, axis=(0, 1))

    partial_sum = stream_part + span_part + wall_part
    pieces = split_wide(partial_sum.T.reshape(gxn, -1))
    extra = jnp.zeros((gxn, nxl - 2, lanes), bf16)
    extra = jnp.concatenate([pieces[0][:, None], pieces[1][:, None], extra], axis=1)
    back = jnp.concatenate([stream_div.reshape(gxn, nxl, comps * lanes), extra], axis=2)
    back = lax.all_to_all(back, "gx", 0, 0, tiled=True)
    summed = jnp.sum(join_wide(back[:, :2, comps * lanes:].transpose(1, 0, 2)), axis=0)
    summed = summed.reshape(ny // gxn, nzl).T
    back = back[:, :, : comps * lanes].reshape(nzl, yparts, nxl, comps, lanes)
    stream_div = back.transpose(3, 2, 0, 1, 4).reshape(comps, nxl, nzl, ny)

    total = stream_div.astype(f32) + wall_div
    total = total + span_div.astype(f32)
    updated = (adjoint.astype(f32) + time_step * total).astype(bf16)

    gradient = -summed / nx
    return (updated, gradient)


def solution(mesh):
    in_specs = (P(None, "gx", "gz", None), P("gx", "gz", None), P("gz", None), P(), P(), P(), P())
    out_specs = (P(None, "gx", "gz", None), P("gz", "gx"))
    return jax.shard_map(
        section, mesh=mesh, in_specs=in_specs, out_specs=out_specs, check_vma=False
    )
```

```python
import jax
import jax.numpy as jnp
from jax import lax
from jax.sharding import PartitionSpec as P

near_coef = 7.0 / 9.0
far_coef = 1.0 / 36.0
time_step = 0.25
f32 = jnp.float32
bf16 = jnp.bfloat16


def folded(operator):
    wide = operator.astype(f32)
    shifted = lambda step: jnp.roll(wide, step, 1)
    merged = near_coef * (shifted(1) - shifted(-1)) + far_coef * (shifted(2) - shifted(-2))
    return split_wide(merged)


def derivative(pencil, operator):
    product = sum(
        jnp.einsum("ij,cjp->cip", part, pencil, preferred_element_type=f32) for part in operator
    )
    return product.astype(bf16)


def xor_order(blocks, mine):
    size = blocks.shape[0]
    return blocks[jnp.bitwise_xor(jnp.arange(size, dtype=jnp.int32), mine)]


def butterfly(blocks, mine):
    size = blocks.shape[0]
    blocks = xor_order(blocks, mine)
    bit = 1
    while bit < size:
        split = blocks.reshape(size // (2 * bit), 2, bit, *blocks.shape[1:])
        pairs = [(src, src ^ bit) for src in range(size)]
        moved = lax.ppermute(split[:, 1], "gz", pairs)
        blocks = jnp.stack([split[:, 0], moved], axis=1).reshape(blocks.shape)
        bit *= 2
    return xor_order(blocks, mine)


def split_wide(value):
    high = lax.reduce_precision(value, exponent_bits=8, mantissa_bits=7)
    return jnp.stack([high.astype(bf16), (value - high).astype(bf16)])


def join_wide(parts):
    return parts[0].astype(f32) + parts[1].astype(f32)


def row_derivative(pencil, operator):
    product = sum(jnp.dot(part, pencil, preferred_element_type=f32) for part in operator)
    return product.astype(bf16)


def wall_derivative(source, wall_operator, metric):
    product = jnp.einsum("kxzj,ij->kxzi", source, wall_operator, preferred_element_type=f32)
    return product * metric


def section(adjoint, strain, correction, metric, stream_inverse, span_inverse, wall_operator):
    comps, nxl, nzl, ny = adjoint.shape
    gxn = lax.axis_size("gx")
    lanes = nzl * ny // gxn
    yparts = ny // lanes
    nx = nxl * gxn
    stream_inverse = folded(stream_inverse)
    span_inverse = folded(span_inverse)
    strain_wide = strain.astype(f32)
    viscosity = (correction[None] * strain_wide).astype(bf16)
    viscous = viscosity.astype(f32)

    xs = jnp.concatenate([adjoint, strain[None]], axis=0)
    xs = xs.reshape(comps + 1, nxl, nzl, yparts, lanes).transpose(2, 3, 1, 0, 4)
    xs = xs.reshape(gxn, nxl, (comps + 1) * lanes)
    xt = lax.all_to_all(xs, "gx", 0, 0, tiled=True)
    xt = xt.reshape(nx, (comps + 1) * lanes)
    stream_strain = xt[:, comps * lanes:].astype(f32)
    me = lax.axis_index("gx")
    z_at, y_at = me // yparts, me % yparts
    corr_row = lax.dynamic_slice(correction, (z_at, y_at * lanes), (1, lanes))
    stream_visc = (corr_row * stream_strain).astype(bf16).astype(f32)
    stream_visc = jnp.tile(stream_visc, (1, comps))
    stream_grad = row_derivative(xt[:, : comps * lanes], stream_inverse)
    stream_flux = (stream_visc * stream_grad.astype(f32)).astype(bf16)
    stream_div = row_derivative(stream_flux, stream_inverse)
    stream_sq = (stream_grad.astype(f32) ** 2).reshape(nx, comps, lanes).sum(axis=1)
    stream_sq = jnp.sum(stream_strain * stream_sq, axis=0)
    z_ids = lax.broadcasted_iota(jnp.int32, (nzl, yparts, lanes), 0)
    y_ids = lax.broadcasted_iota(jnp.int32, (nzl, yparts, lanes), 1)
    owned = (z_ids == z_at) & (y_ids == y_at)
    stream_part = jnp.where(owned, stream_sq[None, None], 0.0).reshape(nzl, ny)

    gzn = lax.axis_size("gz")
    mine = lax.axis_index("gz")
    zs = jnp.concatenate([adjoint, viscosity[None], strain[None]], axis=0)
    zt = lax.all_to_all(zs, "gz", 1, 2, tiled=True)[:, 0]
    span_visc = zt[comps].astype(f32)
    span_strain = zt[comps + 1].astype(f32)
    span_grad = derivative(zt[:comps], span_inverse)
    span_flux = (span_visc[None] * span_grad.astype(f32)).astype(bf16)
    span_div = derivative(span_flux, span_inverse)
    span_sq = jnp.sum(span_strain[None] * span_grad.astype(f32) ** 2, axis=0)
    span_back = jnp.concatenate([span_div, split_wide(span_sq)], axis=0)
    span_back = span_back.reshape(span_back.shape[0], gzn, nzl, ny).transpose(1, 0, 2, 3)
    span_out = butterfly(span_back, mine)
    span_part = jnp.sum(join_wide(span_out[:, comps:].transpose(1, 0, 2, 3)), axis=0)
    span_div = span_out[:, :comps].transpose(1, 0, 2, 3)

    wall_grad = wall_derivative(adjoint, wall_operator, metric).astype(bf16)
    wall_flux = (viscous[None] * wall_grad.astype(f32)).astype(bf16)
    wall_div = wall_derivative(wall_flux, wall_operator, metric)
    wall_part = jnp.sum(strain_wide[None] * wall_grad.astype(f32) ** 2, axis=(0, 1))

    partial_sum = stream_part + span_part + wall_part
    pieces = split_wide(partial_sum.T.reshape(gxn, -1))
    extra = jnp.zeros((gxn, nxl - 2, lanes), bf16)
    extra = jnp.concatenate([pieces[0][:, None], pieces[1][:, None], extra], axis=1)
    back = jnp.concatenate([stream_div.reshape(gxn, nxl, comps * lanes), extra], axis=2)
    back, wall_div = lax.optimization_barrier((back, wall_div))
    back = lax.all_to_all(back, "gx", 0, 0, tiled=True)
    summed = jnp.sum(join_wide(back[:, :2, comps * lanes:].transpose(1, 0, 2)), axis=0)
    summed = summed.reshape(ny // gxn, nzl).T
    back = back[:, :, : comps * lanes].reshape(nzl, yparts, nxl, comps, lanes)
    stream_div = back.transpose(3, 2, 0, 1, 4).reshape(comps, nxl, nzl, ny)

    total = stream_div.astype(f32) + wall_div
    total = total + span_div.astype(f32)
    updated = (adjoint.astype(f32) + time_step * total).astype(bf16)

    gradient = -summed / nx
    return (updated, gradient)


def solution(mesh):
    in_specs = (P(None, "gx", "gz", None), P("gx", "gz", None), P("gz", None), P(), P(), P(), P())
    out_specs = (P(None, "gx", "gz", None), P("gz", "gx"))
    return jax.shard_map(
        section, mesh=mesh, in_specs=in_specs, out_specs=out_specs, check_vma=False
    )
```

```python
import jax
import jax.numpy as jnp
from jax import lax
from jax.sharding import PartitionSpec as P

near_coef = 7.0 / 9.0
far_coef = 1.0 / 36.0
time_step = 0.25
f32 = jnp.float32
bf16 = jnp.bfloat16


def folded(operator):
    wide = operator.astype(f32)
    shifted = lambda step: jnp.roll(wide, step, 1)
    merged = near_coef * (shifted(1) - shifted(-1)) + far_coef * (shifted(2) - shifted(-2))
    return split_wide(merged)


def stencil(source, axis):
    widened = source.astype(f32)
    near_diff = jnp.roll(widened, -1, axis) - jnp.roll(widened, 1, axis)
    far_diff = jnp.roll(widened, -2, axis) - jnp.roll(widened, 2, axis)
    return (near_coef * near_diff + far_coef * far_diff).astype(bf16)


def derivative(pencil, operator):
    right_side = stencil(pencil, 1)
    product = jnp.einsum("ij,cjp->cip", operator, right_side, preferred_element_type=f32)
    return product.astype(bf16)


def xor_order(blocks, mine):
    size = blocks.shape[0]
    return blocks[jnp.bitwise_xor(jnp.arange(size, dtype=jnp.int32), mine)]


def butterfly(blocks, mine):
    size = blocks.shape[0]
    blocks = xor_order(blocks, mine)
    bit = 1
    while bit < size:
        split = blocks.reshape(size // (2 * bit), 2, bit, *blocks.shape[1:])
        pairs = [(src, src ^ bit) for src in range(size)]
        moved = lax.ppermute(split[:, 1], "gz", pairs)
        blocks = jnp.stack([split[:, 0], moved], axis=1).reshape(blocks.shape)
        bit *= 2
    return xor_order(blocks, mine)


def split_wide(value):
    high = lax.reduce_precision(value, exponent_bits=8, mantissa_bits=7)
    return jnp.stack([high.astype(bf16), (value - high).astype(bf16)])


def join_wide(parts):
    return parts[0].astype(f32) + parts[1].astype(f32)


def row_derivative(pencil, operator):
    product = sum(jnp.dot(part, pencil, preferred_element_type=f32) for part in operator)
    return product.astype(bf16)


def wall_derivative(source, wall_operator, metric):
    product = jnp.einsum("kxzj,ij->kxzi", source, wall_operator, preferred_element_type=f32)
    return product * metric


def section(adjoint, strain, correction, metric, stream_inverse, span_inverse, wall_operator):
    comps, nxl, nzl, ny = adjoint.shape
    gxn = lax.axis_size("gx")
    lanes = nzl * ny // gxn
    yparts = ny // lanes
    nx = nxl * gxn
    stream_inverse = folded(stream_inverse)
    strain_wide = strain.astype(f32)
    viscosity = (correction[None] * strain_wide).astype(bf16)
    viscous = viscosity.astype(f32)

    xs = jnp.concatenate([adjoint, strain[None]], axis=0)
    xs = xs.reshape(comps + 1, nxl, nzl, yparts, lanes).transpose(2, 3, 1, 0, 4)
    xs = xs.reshape(gxn, nxl, (comps + 1) * lanes)
    xt = lax.all_to_all(xs, "gx", 0, 0, tiled=True)
    xt = xt.reshape(nx, (comps + 1) * lanes)
    stream_strain = xt[:, comps * lanes:].astype(f32)
    me = lax.axis_index("gx")
    z_at, y_at = me // yparts, me % yparts
    corr_row = lax.dynamic_slice(correction, (z_at, y_at * lanes), (1, lanes))
    stream_visc = (corr_row * stream_strain).astype(bf16).astype(f32)
    stream_visc = jnp.tile(stream_visc, (1, comps))
    stream_grad = row_derivative(xt[:, : comps * lanes], stream_inverse)
    stream_flux = (stream_visc * stream_grad.astype(f32)).astype(bf16)
    stream_div = row_derivative(stream_flux, stream_inverse)
    stream_sq = (stream_grad.astype(f32) ** 2).reshape(nx, comps, lanes).sum(axis=1)
    stream_sq = jnp.sum(stream_strain * stream_sq, axis=0)
    z_ids = lax.broadcasted_iota(jnp.int32, (nzl, yparts, lanes), 0)
    y_ids = lax.broadcasted_iota(jnp.int32, (nzl, yparts, lanes), 1)
    owned = (z_ids == z_at) & (y_ids == y_at)
    stream_part = jnp.where(owned, stream_sq[None, None], 0.0).reshape(nzl, ny)

    gzn = lax.axis_size("gz")
    mine = lax.axis_index("gz")
    zs = jnp.concatenate([adjoint, viscosity[None], strain[None]], axis=0)
    zt = lax.all_to_all(zs, "gz", 1, 2, tiled=True)[:, 0]
    span_visc = zt[comps].astype(f32)
    span_strain = zt[comps + 1].astype(f32)
    span_grad = derivative(zt[:comps], span_inverse)
    span_flux = (span_visc[None] * span_grad.astype(f32)).astype(bf16)
    span_div = derivative(span_flux, span_inverse)
    span_sq = jnp.sum(span_strain[None] * span_grad.astype(f32) ** 2, axis=0)
    span_back = jnp.concatenate([span_div, split_wide(span_sq)], axis=0)
    span_back = span_back.reshape(span_back.shape[0], gzn, nzl, ny).transpose(1, 0, 2, 3)
    span_out = butterfly(span_back, mine)
    span_part = jnp.sum(join_wide(span_out[:, comps:].transpose(1, 0, 2, 3)), axis=0)
    span_div = span_out[:, :comps].transpose(1, 0, 2, 3)

    wall_grad = wall_derivative(adjoint, wall_operator, metric).astype(bf16)
    wall_flux = (viscous[None] * wall_grad.astype(f32)).astype(bf16)
    wall_div = wall_derivative(wall_flux, wall_operator, metric)
    wall_part = jnp.sum(strain_wide[None] * wall_grad.astype(f32) ** 2, axis=(0, 1))

    partial_sum = stream_part + span_part + wall_part
    pieces = split_wide(partial_sum.T.reshape(gxn, -1))
    extra = jnp.zeros((gxn, nxl - 2, lanes), bf16)
    extra = jnp.concatenate([pieces[0][:, None], pieces[1][:, None], extra], axis=1)
    back = jnp.concatenate([stream_div.reshape(gxn, nxl, comps * lanes), extra], axis=2)
    back, wall_div = lax.optimization_barrier((back, wall_div))
    back = lax.all_to_all(back, "gx", 0, 0, tiled=True)
    summed = jnp.sum(join_wide(back[:, :2, comps * lanes:].transpose(1, 0, 2)), axis=0)
    summed = summed.reshape(ny // gxn, nzl).T
    back = back[:, :, : comps * lanes].reshape(nzl, yparts, nxl, comps, lanes)
    stream_div = back.transpose(3, 2, 0, 1, 4).reshape(comps, nxl, nzl, ny)

    total = stream_div.astype(f32) + wall_div
    total = total + span_div.astype(f32)
    updated = (adjoint.astype(f32) + time_step * total).astype(bf16)

    gradient = -summed / nx
    return (updated, gradient)


def solution(mesh):
    in_specs = (P(None, "gx", "gz", None), P("gx", "gz", None), P("gz", None), P(), P(), P(), P())
    out_specs = (P(None, "gx", "gz", None), P("gz", "gx"))
    return jax.shard_map(
        section, mesh=mesh, in_specs=in_specs, out_specs=out_specs, check_vma=False
    )
```

```python
import jax
import jax.numpy as jnp
from jax import lax
from jax.sharding import PartitionSpec as P

near_coef = 7.0 / 9.0
far_coef = 1.0 / 36.0
time_step = 0.25
f32 = jnp.float32
bf16 = jnp.bfloat16


def folded(operator):
    wide = operator.astype(f32)
    shifted = lambda step: jnp.roll(wide, step, 1)
    merged = near_coef * (shifted(1) - shifted(-1)) + far_coef * (shifted(2) - shifted(-2))
    return split_wide(merged)


def stencil(source, axis):
    widened = source.astype(f32)
    near_diff = jnp.roll(widened, -1, axis) - jnp.roll(widened, 1, axis)
    far_diff = jnp.roll(widened, -2, axis) - jnp.roll(widened, 2, axis)
    return (near_coef * near_diff + far_coef * far_diff).astype(bf16)


def derivative(pencil, operator):
    right_side = stencil(pencil, 1)
    product = jnp.einsum("ij,cjp->cip", operator, right_side, preferred_element_type=f32)
    return product.astype(bf16)


def xor_order(blocks, mine):
    size = blocks.shape[0]
    return blocks[jnp.bitwise_xor(jnp.arange(size, dtype=jnp.int32), mine)]


def butterfly(blocks, mine):
    size = blocks.shape[0]
    blocks = xor_order(blocks, mine)
    bit = 1
    while bit < size:
        split = blocks.reshape(size // (2 * bit), 2, bit, *blocks.shape[1:])
        pairs = [(src, src ^ bit) for src in range(size)]
        moved = lax.ppermute(split[:, 1], "gz", pairs)
        blocks = jnp.stack([split[:, 0], moved], axis=1).reshape(blocks.shape)
        bit *= 2
    return xor_order(blocks, mine)


def split_wide(value):
    high = lax.reduce_precision(value, exponent_bits=8, mantissa_bits=7)
    return jnp.stack([high.astype(bf16), (value - high).astype(bf16)])


def join_wide(parts):
    return parts[0].astype(f32) + parts[1].astype(f32)


def row_derivative(pencil, operator):
    product = sum(jnp.dot(part, pencil, preferred_element_type=f32) for part in operator)
    return product.astype(bf16)


def wall_derivative(source, wall_operator, metric):
    product = jnp.einsum("kxzj,ij->kxzi", source, wall_operator, preferred_element_type=f32)
    return product * metric


def section(adjoint, strain, correction, metric, stream_inverse, span_inverse, wall_operator):
    comps, nxl, nzl, ny = adjoint.shape
    gxn = lax.axis_size("gx")
    lanes = nzl * ny // gxn
    yparts = ny // lanes
    nx = nxl * gxn
    stream_inverse = folded(stream_inverse)
    strain_wide = strain.astype(f32)
    viscosity = (correction[None] * strain_wide).astype(bf16)
    viscous = viscosity.astype(f32)

    xs = jnp.concatenate([adjoint, strain[None]], axis=0)
    xs = xs.reshape(comps + 1, nxl, nzl, yparts, lanes).transpose(2, 3, 1, 0, 4)
    xs = xs.reshape(gxn, nxl, (comps + 1) * lanes)
    xt = lax.all_to_all(xs, "gx", 0, 0, tiled=True)
    xt = xt.reshape(nx, (comps + 1) * lanes)
    stream_strain = xt[:, comps * lanes:].astype(f32)
    me = lax.axis_index("gx")
    z_at, y_at = me // yparts, me % yparts
    corr_row = lax.dynamic_slice(correction, (z_at, y_at * lanes), (1, lanes))
    stream_visc = (corr_row * stream_strain).astype(bf16).astype(f32)
    stream_visc = jnp.tile(stream_visc, (1, comps))
    stream_grad = row_derivative(xt[:, : comps * lanes], stream_inverse)
    stream_flux = (stream_visc * stream_grad.astype(f32)).astype(bf16)
    stream_div = row_derivative(stream_flux, stream_inverse)
    stream_sq = (stream_grad.astype(f32) ** 2).reshape(nx, comps, lanes).sum(axis=1)
    stream_sq = jnp.sum(stream_strain * stream_sq, axis=0)
    z_ids = lax.broadcasted_iota(jnp.int32, (nzl, yparts, lanes), 0)
    y_ids = lax.broadcasted_iota(jnp.int32, (nzl, yparts, lanes), 1)
    owned = (z_ids == z_at) & (y_ids == y_at)
    stream_part = jnp.where(owned, stream_sq[None, None], 0.0).reshape(nzl, ny)

    gzn = lax.axis_size("gz")
    mine = lax.axis_index("gz")
    zs = jnp.concatenate([adjoint, viscosity[None], strain[None]], axis=0)
    zt = lax.all_to_all(zs, "gz", 1, 2, tiled=True)
    zt = zt[:, 0]
    span_visc = zt[comps].astype(f32)
    span_strain = zt[comps + 1].astype(f32)
    span_grad = derivative(zt[:comps], span_inverse)
    span_flux = (span_visc[None] * span_grad.astype(f32)).astype(bf16)
    span_div = derivative(span_flux, span_inverse)
    span_sq = jnp.sum(span_strain[None] * span_grad.astype(f32) ** 2, axis=0)
    span_back = jnp.concatenate([span_div, split_wide(span_sq)], axis=0)
    span_back = span_back.reshape(span_back.shape[0], gzn, nzl, ny).transpose(1, 0, 2, 3)
    span_out = butterfly(span_back, mine)
    span_part = jnp.sum(join_wide(span_out[:, comps:].transpose(1, 0, 2, 3)), axis=0)
    span_div = span_out[:, :comps].transpose(1, 0, 2, 3)

    wall_grad = wall_derivative(adjoint, wall_operator, metric).astype(bf16)
    wall_flux = (viscous[None] * wall_grad.astype(f32)).astype(bf16)
    wall_div = wall_derivative(wall_flux, wall_operator, metric)
    wall_part = jnp.sum(strain_wide[None] * wall_grad.astype(f32) ** 2, axis=(0, 1))

    other_part = lax.optimization_barrier(span_part + wall_part)
    partial_sum = stream_part + other_part
    pieces = split_wide(partial_sum.T.reshape(gxn, -1))
    extra = jnp.zeros((gxn, nxl - 2, lanes), bf16)
    extra = jnp.concatenate([pieces[0][:, None], pieces[1][:, None], extra], axis=1)
    back = jnp.concatenate([stream_div.reshape(gxn, nxl, comps * lanes), extra], axis=2)
    back, wall_div = lax.optimization_barrier((back, wall_div))
    back = lax.all_to_all(back, "gx", 0, 0, tiled=True)
    summed = jnp.sum(join_wide(back[:, :2, comps * lanes:].transpose(1, 0, 2)), axis=0)
    summed = summed.reshape(ny // gxn, nzl).T
    back = back[:, :, : comps * lanes].reshape(nzl, yparts, nxl, comps, lanes)
    stream_div = back.transpose(3, 2, 0, 1, 4).reshape(comps, nxl, nzl, ny)

    total = stream_div.astype(f32) + wall_div
    total = total + span_div.astype(f32)
    updated = (adjoint.astype(f32) + time_step * total).astype(bf16)

    gradient = -summed / nx
    return (updated, gradient)


def solution(mesh):
    in_specs = (P(None, "gx", "gz", None), P("gx", "gz", None), P("gz", None), P(), P(), P(), P())
    out_specs = (P(None, "gx", "gz", None), P("gz", "gx"))
    return jax.shard_map(
        section, mesh=mesh, in_specs=in_specs, out_specs=out_specs, check_vma=False
    )
```
